512 devices in a mesh: frame: 16 (over z_lo, y), space: 32 (over z_hi, x, core).
Axes of the slice: x: 4, y: 8, z: 8 (z_hi: 4, z_lo: 2; z = z_hi * 2 + z_lo), core: 2. Of those that a mesh axis runs over, the one named last changes fastest.
Arguments:
- features: bfloat16 [16, 64, 512, 256], P('frame', None, 'space'), may hold values from -6 to 6
- enc_w: bfloat16 [3, 3, 64, 64], replicated, may hold values from -0.25 to 0.25
- enc_b: float32 [64], replicated, may hold values from -3 to 3
- mix_w: bfloat16 [128, 1024], replicated, may hold values from -0.1875 to 0.1875
- mix_b: float32 [128], replicated, may hold values from -3 to 3
- branch3: bfloat16 [3, 3, 1024, 16], P(None, None, 'frame'), may hold values from -0.5 to 0.5
- branch5: bfloat16 [5, 5, 1024, 16], P(None, None, 'frame'), may hold values from -0.3125 to 0.3125
- branch7: bfloat16 [7, 7, 1024, 16], P(None, None, 'frame'), may hold values from -0.21875 to 0.21875
- branch11: bfloat16 [11, 11, 1024, 16], P(None, None, 'frame'), may hold values from -0.125 to 0.125
- branch_b: float32 [4, 1024], P(None, 'frame'), may hold values from -3 to 3
- dec_w: bfloat16 [3, 3, 64, 64], replicated, may hold values from -0.25 to 0.25
- dec_b: float32 [64], replicated, may hold values from -3 to 3
Outputs:
- decoded: bfloat16 [16, 64, 512, 256], P('frame', None, 'space')
The draws below stay inside these ranges and needn't reach their ends.
All inputs are finite; a program needn't handle non-finite values.
Results may differ from the reference program's by a relative error of at most 0.019.
Values may be sent and summed in bfloat16 or wider, within the bound.
No kernel may reach another device: no remote copies, remote signals or barrier semaphores. Data moves between devices by JAX's collectives and lax.ppermute only.
A program may use at most 64 MiB of HBM per device.

```python
import jax
import jax.numpy as jnp
from jax import lax

C = 64
HID = 128
GROUPS = 8
F = 16
H = 512
W = 256
OUT = 1024


def steps_of(stream_key, shape, shards, smallest, largest):
    loudness, own = 1.0, jax.random.fold_in(stream_key, 6)
    for dim, parts in shards:
        steps = jnp.exp(jax.random.uniform(jax.random.fold_in(own, dim), (parts,), jnp.float32, smallest / len(shards), largest / len(shards)))
        loudness = loudness * jnp.repeat(steps, shape[dim] // parts).reshape([-1 if axis == dim else 1 for axis in range(len(shape))])
    return loudness


def gaussian(key, dims, spread, most, pieces=(), dtype=jnp.bfloat16):
    gain = steps_of(key, dims, pieces, -0.22, 0.18) if pieces else 1.0
    values = jax.random.normal(key, dims, jnp.float32) * spread * gain
    return jnp.minimum(jnp.maximum(values, -most), most).astype(dtype)


def setup_inputs(seed: int = 0) -> dict:
    key_list = jax.random.split(jax.random.key(seed), 13)
    features = gaussian(key_list[0], (F, C, H, W), 1.0, 6.0, ((0, 16), (2, 32)))
    enc_w = gaussian(key_list[1], (3, 3, C, C), (9 * C) ** -0.5, 0.25)
    enc_b = gaussian(key_list[2], (C,), 0.5, 3.0, (), jnp.float32)
    mix_w = gaussian(key_list[3], (HID, OUT), OUT ** -0.5, 0.1875)
    mix_b = gaussian(key_list[4], (HID,), 0.5, 3.0, (), jnp.float32)
    branch3 = gaussian(key_list[5], (3, 3, OUT, HID // GROUPS), (9 * (HID // GROUPS)) ** -0.5, 0.5, ((2, 16),))
    branch5 = gaussian(key_list[6], (5, 5, OUT, HID // GROUPS), (25 * (HID // GROUPS)) ** -0.5, 0.3125, ((2, 16),))
    branch7 = gaussian(key_list[7], (7, 7, OUT, HID // GROUPS), (49 * (HID // GROUPS)) ** -0.5, 0.21875, ((2, 16),))
    branch11 = gaussian(key_list[8], (11, 11, OUT, HID // GROUPS), (121 * (HID // GROUPS)) ** -0.5, 0.125, ((2, 16),))
    branch_b = gaussian(key_list[9], (4, OUT), 0.5, 3.0, ((1, 16),), jnp.float32)
    dec_w = gaussian(key_list[10], (3, 3, C, C), (9 * C) ** -0.5, 0.25)
    dec_b = gaussian(key_list[11], (C,), 0.5, 3.0, (), jnp.float32)
    return dict(features=features, enc_w=enc_w, enc_b=enc_b, mix_w=mix_w, mix_b=mix_b, branch3=branch3, branch5=branch5, branch7=branch7, branch11=branch11, branch_b=branch_b, dec_w=dec_w, dec_b=dec_b)


def conv_same(values, kernel, width, group_count):
    oihw = jnp.transpose(kernel.astype(jnp.float32), (2, 3, 0, 1))
    half = width // 2
    return lax.conv_general_dilated(values, oihw, (1, 1), ((half, half), (half, half)),
                                    dimension_numbers=("NCHW", "OIHW", "NCHW"),
                                    feature_group_count=group_count,
                                    precision=lax.Precision.HIGHEST)


def reference(features, enc_w, enc_b, mix_w, mix_b, branch3, branch5, branch7, branch11, branch_b, dec_w, dec_b):
    encoded = jax.nn.silu(conv_same(features.astype(jnp.float32), enc_w, 3, 1) + enc_b[None, :, None, None]).astype(jnp.bfloat16)
    frames, channels, row_count, col_count = encoded.shape
    stacked = encoded.reshape(frames * channels, row_count, col_count).astype(jnp.float32)
    hidden = (jnp.einsum("ji,irw->jrw", mix_w.astype(jnp.float32), stacked, precision=lax.Precision.HIGHEST)
              + mix_b[:, None, None]).astype(jnp.bfloat16)
    hidden_batch = hidden.astype(jnp.float32)[None]
    summed = jnp.zeros((frames * channels, row_count, col_count), jnp.float32)
    for branch_index, (width, kernel) in enumerate(((3, branch3), (5, branch5), (7, branch7), (11, branch11))):
        branch = conv_same(hidden_batch, kernel, width, GROUPS)[0] + branch_b[branch_index][:, None, None]
        summed = summed + jnp.where(branch > 0, branch, 0.2 * branch)
    joined = (summed.reshape(frames, channels, row_count, col_count) + encoded.astype(jnp.float32)).astype(jnp.bfloat16)
    return jax.nn.silu(conv_same(joined.astype(jnp.float32), dec_w, 3, 1) + dec_b[None, :, None, None]).astype(jnp.bfloat16)
```

```python
import jax
import jax.numpy as jnp
from jax import lax
from jax.sharding import PartitionSpec as P

GROUPS = 8


def padded_2(block, sides, width):
    for axis, dim in sides:
        count = lax.axis_size(axis)
        forward = [(i, i + 1) for i in range(count - 1)]
        backward = [(target, source) for source, target in forward]
        low = lax.ppermute(
            lax.slice_in_dim(block, block.shape[dim] - width, None, axis=dim), axis, forward
        )
        high = lax.ppermute(lax.slice_in_dim(block, 0, width, axis=dim), axis, backward)
        block = jnp.concatenate([low, block, high], axis=dim)
    return block


def halving_sum(partial, frame_index, frames, group_width):
    share = frames // GROUPS
    bits = GROUPS.bit_length() - 1
    group_index = frame_index // share
    blocks = partial.reshape((2,) * bits + (group_width,) + partial.shape[1:])
    order = [bits - 1] + list(range(bits - 1))
    axis_of = {bit: bits - 1 - bit for bit in range(bits)}
    for position, bit in enumerate(order):
        axis = axis_of[bit] - sum(1 for done in order[:position] if axis_of[done] < axis_of[bit])
        mine = (group_index >> bit) & 1
        keep = lax.dynamic_index_in_dim(blocks, mine, axis, keepdims=False)
        send = lax.dynamic_index_in_dim(blocks, 1 - mine, axis, keepdims=False)
        step = share << bit
        pairs = [(i, i ^ step) for i in range(frames)]
        got = lax.ppermute(send.astype(jnp.bfloat16), "frame", pairs)
        blocks = keep + got.astype(jnp.float32)
    step = 1
    while step < share:
        pairs = [(i, i ^ step) for i in range(frames)]
        got = lax.ppermute(blocks.astype(jnp.bfloat16), "frame", pairs)
        blocks = blocks.astype(jnp.bfloat16).astype(jnp.float32) + got.astype(jnp.float32)
        step *= 2
    return blocks


def sweep(padded, weight, kernel_size, start, row_count, col_count):
    summed = jnp.zeros((padded.shape[0], weight.shape[3], row_count, col_count), jnp.float32)
    for row_tap in range(kernel_size):
        band = lax.slice_in_dim(padded, start + row_tap, start + row_tap + row_count, axis=2)
        window = jnp.stack(
            [
                lax.slice_in_dim(band, start + col_tap, start + col_tap + col_count, axis=3)
                for col_tap in range(kernel_size)
            ],
            axis=2,
        )
        summed = summed + jnp.einsum(
            "dgoi,gidrw->gorw", weight[row_tap], window, preferred_element_type=jnp.float32
        )
    return summed


def finish(padded, weight, bias, row_count, col_count):
    padded = jnp.pad(padded, ((0, 0), (0, 0), (0, 0), (1, 1)))
    summed = sweep(padded, weight[:, :, None], 3, 0, row_count, col_count)
    return jax.nn.silu(summed + bias[None, :, None, None]).astype(jnp.bfloat16)


def per_device(
    features,
    enc_w,
    enc_b,
    mix_w,
    mix_b,
    branch3,
    branch5,
    branch7,
    branch11,
    branch_b,
    dec_w,
    dec_b,
):
    frame_index = lax.axis_index("frame")
    frames = lax.axis_size("frame")
    channels, row_count, col_count = (features.shape[1], features.shape[2], features.shape[3])
    padded = padded_2(features, (("space", 2),), 1)
    encoded = finish(padded, enc_w, enc_b, row_count, col_count)
    hidden_count = mix_w.shape[0]
    frame_weight = lax.dynamic_slice_in_dim(mix_w, frame_index * channels, channels, 1)
    partial_mix = jnp.einsum(
        "ji,irw->jrw", frame_weight, encoded[0], preferred_element_type=jnp.float32
    )
    per_group = frames * channels // GROUPS
    group_width = hidden_count // GROUPS
    local_groups = max(1, channels // per_group)
    own_groups = (
        halving_sum(partial_mix, frame_index, frames, group_width)
        + lax.dynamic_slice_in_dim(
            mix_b, (frame_index * channels // per_group) * group_width, group_width
        )[:, None, None]
    ).astype(jnp.bfloat16)
    margin = padded_2(own_groups, (("space", 1),), 5)
    margin = jnp.pad(margin, ((0, 0), (0, 0), (5, 5)))
    group_block = margin.reshape(local_groups, group_width, row_count + 10, col_count + 10)
    summed = jnp.zeros((channels, row_count, col_count), jnp.float32)
    for branch_index, weight in enumerate((branch3, branch5, branch7, branch11)):
        kernel_size = weight.shape[0]
        shaped = weight.reshape(
            kernel_size, kernel_size, local_groups, channels // local_groups, group_width
        )
        branch = sweep(group_block, shaped, kernel_size, 5 - kernel_size // 2, row_count, col_count)
        branch = (
            branch.reshape(channels, row_count, col_count) + branch_b[branch_index][:, None, None]
        )
        summed = summed + jnp.where(branch > 0, branch, 0.2 * branch)
    joined = (summed + encoded[0].astype(jnp.float32)).astype(jnp.bfloat16)[None]
    padded_dec = padded_2(joined, (("space", 2),), 1)
    return finish(padded_dec, dec_w, dec_b, row_count, col_count)


def solution(mesh):
    placed = (
        P("frame", None, "space", None),
        P(),
        P(),
        P(),
        P(),
        P(None, None, "frame", None),
        P(None, None, "frame", None),
        P(None, None, "frame", None),
        P(None, None, "frame", None),
        P(None, "frame"),
        P(),
        P(),
    )
    return jax.shard_map(
        per_device,
        mesh=mesh,
        in_specs=placed,
        out_specs=P("frame", None, "space", None),
        check_vma=False,
    )
```

```python
import jax
import jax.numpy as jnp
from jax import lax
from jax.sharding import PartitionSpec as P

GROUPS = 8


def padded_2(block, sides, width):
    for axis, dim in sides:
        count = lax.axis_size(axis)
        forward = [(i, i + 1) for i in range(count - 1)]
        backward = [(target, source) for source, target in forward]
        low = lax.ppermute(
            lax.slice_in_dim(block, block.shape[dim] - width, None, axis=dim), axis, forward
        )
        high = lax.ppermute(lax.slice_in_dim(block, 0, width, axis=dim), axis, backward)
        block = jnp.concatenate([low, block, high], axis=dim)
    return block


def project(encoded, mix_w, mix_b, frames, group_width):
    channels, row_count, col_count = encoded.shape
    rows = row_count // frames
    blocks = encoded.reshape(channels, frames, rows, col_count).transpose(1, 0, 2, 3)
    stacked = lax.all_to_all(blocks, "frame", 0, 0, tiled=False)
    stacked = stacked.reshape(frames * channels, rows, col_count)
    hidden = (
        jnp.einsum("ji,irw->jrw", mix_w, stacked, preferred_element_type=jnp.float32)
        + mix_b[:, None, None]
    ).astype(jnp.bfloat16)
    hidden = hidden.reshape(GROUPS, group_width, rows, col_count)
    hidden = jnp.repeat(hidden, frames // GROUPS, axis=0)
    own = lax.all_to_all(hidden, "frame", 0, 0, tiled=False)
    return own.transpose(1, 0, 2, 3).reshape(group_width, row_count, col_count)


def sweep(padded, weight, kernel_size, start, row_count, col_count):
    summed = jnp.zeros((padded.shape[0], weight.shape[3], row_count, col_count), jnp.float32)
    for row_tap in range(kernel_size):
        band = lax.slice_in_dim(padded, start + row_tap, start + row_tap + row_count, axis=2)
        window = jnp.stack(
            [
                lax.slice_in_dim(band, start + col_tap, start + col_tap + col_count, axis=3)
                for col_tap in range(kernel_size)
            ],
            axis=2,
        )
        summed = summed + jnp.einsum(
            "dgoi,gidrw->gorw", weight[row_tap], window, preferred_element_type=jnp.float32
        )
    return summed


def finish(padded, weight, bias, row_count, col_count):
    padded = jnp.pad(padded, ((0, 0), (0, 0), (0, 0), (1, 1)))
    summed = sweep(padded, weight[:, :, None], 3, 0, row_count, col_count)
    return jax.nn.silu(summed + bias[None, :, None, None]).astype(jnp.bfloat16)


def per_device(
    features,
    enc_w,
    enc_b,
    mix_w,
    mix_b,
    branch3,
    branch5,
    branch7,
    branch11,
    branch_b,
    dec_w,
    dec_b,
):
    frame_index = lax.axis_index("frame")
    frames = lax.axis_size("frame")
    channels, row_count, col_count = (features.shape[1], features.shape[2], features.shape[3])
    padded = padded_2(features, (("space", 2),), 1)
    encoded = finish(padded, enc_w, enc_b, row_count, col_count)
    hidden_count = mix_w.shape[0]
    per_group = frames * channels // GROUPS
    group_width = hidden_count // GROUPS
    local_groups = max(1, channels // per_group)
    own_groups = project(encoded[0], mix_w, mix_b, frames, group_width)
    margin = padded_2(own_groups, (("space", 1),), 5)
    margin = jnp.pad(margin, ((0, 0), (0, 0), (5, 5)))
    group_block = margin.reshape(local_groups, group_width, row_count + 10, col_count + 10)
    summed = jnp.zeros((channels, row_count, col_count), jnp.float32)
    for branch_index, weight in enumerate((branch3, branch5, branch7, branch11)):
        kernel_size = weight.shape[0]
        shaped = weight.reshape(
            kernel_size, kernel_size, local_groups, channels // local_groups, group_width
        )
        branch = sweep(group_block, shaped, kernel_size, 5 - kernel_size // 2, row_count, col_count)
        branch = (
            branch.reshape(channels, row_count, col_count) + branch_b[branch_index][:, None, None]
        )
        summed = summed + jnp.where(branch > 0, branch, 0.2 * branch)
    joined = (summed + encoded[0].astype(jnp.float32)).astype(jnp.bfloat16)[None]
    padded_dec = padded_2(joined, (("space", 2),), 1)
    return finish(padded_dec, dec_w, dec_b, row_count, col_count)


def solution(mesh):
    placed = (
        P("frame", None, "space", None),
        P(),
        P(),
        P(),
        P(),
        P(None, None, "frame", None),
        P(None, None, "frame", None),
        P(None, None, "frame", None),
        P(None, None, "frame", None),
        P(None, "frame"),
        P(),
        P(),
    )
    return jax.shard_map(
        per_device,
        mesh=mesh,
        in_specs=placed,
        out_specs=P("frame", None, "space", None),
        check_vma=False,
    )
```

```python
import functools

import jax
import jax.numpy as jnp
from jax.experimental import pallas as pl
from jax import lax
from jax.sharding import PartitionSpec as P

GROUPS = 8


def padded_2(block, sides, width):
    for axis, dim in sides:
        count = lax.axis_size(axis)
        forward = [(i, i + 1) for i in range(count - 1)]
        backward = [(target, source) for source, target in forward]
        low = lax.ppermute(
            lax.slice_in_dim(block, block.shape[dim] - width, None, axis=dim), axis, forward
        )
        high = lax.ppermute(lax.slice_in_dim(block, 0, width, axis=dim), axis, backward)
        block = jnp.concatenate([low, block, high], axis=dim)
    return block


def project(encoded, mix_w, mix_b, frames, group_width):
    channels, row_count, col_count = encoded.shape
    rows = row_count // frames
    blocks = encoded.reshape(channels, frames, rows, col_count).transpose(1, 0, 2, 3)
    stacked = lax.all_to_all(blocks, "frame", 0, 0, tiled=False)
    stacked = stacked.reshape(frames * channels, rows, col_count)
    hidden = (
        jnp.einsum("ji,irw->jrw", mix_w, stacked, preferred_element_type=jnp.float32)
        + mix_b[:, None, None]
    ).astype(jnp.bfloat16)
    hidden = hidden.reshape(GROUPS, group_width, rows, col_count)
    hidden = jnp.repeat(hidden, frames // GROUPS, axis=0)
    own = lax.all_to_all(hidden, "frame", 0, 0, tiled=False)
    return own.transpose(1, 0, 2, 3).reshape(group_width, row_count, col_count)


def branch_kernel(window_ref, weight_ref, bias_ref, out_ref, *, row_count, row_pitch, taps, width):
    def row(y, carry):
        acc = jnp.zeros((row_pitch, weight_ref.shape[2]), jnp.float32)
        for tap in range(taps):
            start = pl.multiple_of((y + tap) * row_pitch, 16)
            acc = acc + jnp.dot(
                window_ref[pl.ds(start, row_pitch), :],
                weight_ref[tap],
                preferred_element_type=jnp.float32,
            )
        acc = acc + bias_ref[...]
        acc = jnp.where(acc > 0, acc, 0.2 * acc)
        total = acc[:, 0:width]
        for part in range(1, weight_ref.shape[2] // width):
            total = total + acc[:, part * width : (part + 1) * width]
        out_ref[pl.ds(pl.multiple_of(y * row_pitch, 16), row_pitch), :] = total
        return carry

    lax.fori_loop(0, row_count, row, 0)


def branches(margin, weights, biases, row_count, col_count):
    inner = margin.shape[0]
    taps = max(w.shape[0] for w in weights)
    half = taps // 2
    out_width = weights[0].shape[2]
    row_pitch = -(-(col_count + 2 * half) // 16) * 16
    padded = jnp.pad(margin, ((0, 0), (0, 0), (half, row_pitch - col_count - half)))
    flat = padded.transpose(1, 2, 0).reshape(-1, inner)
    length = flat.shape[0]
    flat = jnp.pad(flat, ((0, 16), (0, 0)))
    window = jnp.concatenate([flat[shift : shift + length] for shift in range(taps)], axis=1)
    stacked = []
    for w in weights:
        k = w.shape[0]
        low = half - k // 2
        w = jnp.pad(w, ((low, taps - k - low), (low, taps - k - low), (0, 0), (0, 0)))
        stacked.append(w.transpose(0, 1, 3, 2).reshape(taps, taps * inner, out_width))
    weight = jnp.concatenate(stacked, axis=2)
    bias = biases.reshape(1, -1)
    out = pl.pallas_call(
        functools.partial(
            branch_kernel, row_count=row_count, row_pitch=row_pitch, taps=taps, width=out_width
        ),
        out_shape=jax.ShapeDtypeStruct((row_count * row_pitch, out_width), jnp.float32),
    )(window, weight, bias)
    out = out.reshape(row_count, row_pitch, out_width)[:, :col_count]
    return out.transpose(2, 0, 1)


def sweep(padded, weight, kernel_size, start, row_count, col_count):
    summed = jnp.zeros((padded.shape[0], weight.shape[3], row_count, col_count), jnp.float32)
    for row_tap in range(kernel_size):
        band = lax.slice_in_dim(padded, start + row_tap, start + row_tap + row_count, axis=2)
        window = jnp.stack(
            [
                lax.slice_in_dim(band, start + col_tap, start + col_tap + col_count, axis=3)
                for col_tap in range(kernel_size)
            ],
            axis=2,
        )
        summed = summed + jnp.einsum(
            "dgoi,gidrw->gorw", weight[row_tap], window, preferred_element_type=jnp.float32
        )
    return summed


def finish(padded, weight, bias, row_count, col_count):
    padded = jnp.pad(padded, ((0, 0), (0, 0), (0, 0), (1, 1)))
    summed = sweep(padded, weight[:, :, None], 3, 0, row_count, col_count)
    return jax.nn.silu(summed + bias[None, :, None, None]).astype(jnp.bfloat16)


def per_device(
    features,
    enc_w,
    enc_b,
    mix_w,
    mix_b,
    branch3,
    branch5,
    branch7,
    branch11,
    branch_b,
    dec_w,
    dec_b,
):
    frame_index = lax.axis_index("frame")
    frames = lax.axis_size("frame")
    channels, row_count, col_count = (features.shape[1], features.shape[2], features.shape[3])
    padded = padded_2(features, (("space", 2),), 1)
    encoded = finish(padded, enc_w, enc_b, row_count, col_count)
    hidden_count = mix_w.shape[0]
    per_group = frames * channels // GROUPS
    group_width = hidden_count // GROUPS
    local_groups = max(1, channels // per_group)
    own_groups = project(encoded[0], mix_w, mix_b, frames, group_width)
    margin = padded_2(own_groups, (("space", 1),), 5)
    summed = branches(margin, (branch3, branch5, branch7, branch11), branch_b, row_count, col_count)
    joined = (summed + encoded[0].astype(jnp.float32)).astype(jnp.bfloat16)[None]
    padded_dec = padded_2(joined, (("space", 2),), 1)
    return finish(padded_dec, dec_w, dec_b, row_count, col_count)


def solution(mesh):
    placed = (
        P("frame", None, "space", None),
        P(),
        P(),
        P(),
        P(),
        P(None, None, "frame", None),
        P(None, None, "frame", None),
        P(None, None, "frame", None),
        P(None, None, "frame", None),
        P(None, "frame"),
        P(),
        P(),
    )
    return jax.shard_map(
        per_device,
        mesh=mesh,
        in_specs=placed,
        out_specs=P("frame", None, "space", None),
        check_vma=False,
    )
```

```python
import jax
import jax.numpy as jnp
from jax import lax
from jax.sharding import PartitionSpec as P

GROUPS = 8


def padded_2(block, sides, width):
    for axis, dim in sides:
        count = lax.axis_size(axis)
        forward = [(i, i + 1) for i in range(count - 1)]
        backward = [(target, source) for source, target in forward]
        low = lax.ppermute(
            lax.slice_in_dim(block, block.shape[dim] - width, None, axis=dim), axis, forward
        )
        high = lax.ppermute(lax.slice_in_dim(block, 0, width, axis=dim), axis, backward)
        block = jnp.concatenate([low, block, high], axis=dim)
    return block


def project(encoded, mix_w, mix_b, frames, group_width):
    channels, row_count, col_count = encoded.shape
    rows = row_count // frames
    blocks = encoded.reshape(channels, frames, rows, col_count).transpose(1, 0, 2, 3)
    stacked = lax.all_to_all(blocks, "frame", 0, 0, tiled=False)
    stacked = stacked.reshape(frames * channels, rows, col_count)
    hidden = (
        jnp.einsum("ji,irw->jrw", mix_w, stacked, preferred_element_type=jnp.float32)
        + mix_b[:, None, None]
    ).astype(jnp.bfloat16)
    hidden = hidden.reshape(GROUPS, group_width, rows, col_count)
    hidden = jnp.repeat(hidden, frames // GROUPS, axis=0)
    own = lax.all_to_all(hidden, "frame", 0, 0, tiled=False)
    return own.transpose(1, 0, 2, 3).reshape(group_width, row_count, col_count)


def branches(margin, weights, biases, row_count, col_count):
    half = max(w.shape[0] for w in weights) // 2
    shifted = jnp.stack(
        [lax.slice_in_dim(margin, b, b + col_count, axis=2) for b in range(2 * half + 1)]
    )
    summed = jnp.zeros((weights[0].shape[2], row_count, col_count), jnp.float32)
    for index, weight in enumerate(weights):
        k = weight.shape[0]
        low = half - k // 2
        acc = jnp.zeros_like(summed)
        for a in range(k):
            window = lax.slice_in_dim(shifted, low, low + k, axis=0)
            window = lax.slice_in_dim(window, low + a, low + a + row_count, axis=2)
            acc = acc + jnp.einsum(
                "doi,dirw->orw", weight[a], window, preferred_element_type=jnp.float32
            )
        acc = acc + biases[index][:, None, None]
        summed = summed + jnp.where(acc > 0, acc, 0.2 * acc)
    return summed


def sweep(padded, weight, kernel_size, start, row_count, col_count):
    summed = jnp.zeros((padded.shape[0], weight.shape[3], row_count, col_count), jnp.float32)
    for row_tap in range(kernel_size):
        band = lax.slice_in_dim(padded, start + row_tap, start + row_tap + row_count, axis=2)
        window = jnp.stack(
            [
                lax.slice_in_dim(band, start + col_tap, start + col_tap + col_count, axis=3)
                for col_tap in range(kernel_size)
            ],
            axis=2,
        )
        summed = summed + jnp.einsum(
            "dgoi,gidrw->gorw", weight[row_tap], window, preferred_element_type=jnp.float32
        )
    return summed


def finish(padded, weight, bias, row_count, col_count):
    padded = jnp.pad(padded, ((0, 0), (0, 0), (0, 0), (1, 1)))
    summed = sweep(padded, weight[:, :, None], 3, 0, row_count, col_count)
    return jax.nn.silu(summed + bias[None, :, None, None]).astype(jnp.bfloat16)


def per_device(
    features,
    enc_w,
    enc_b,
    mix_w,
    mix_b,
    branch3,
    branch5,
    branch7,
    branch11,
    branch_b,
    dec_w,
    dec_b,
):
    frame_index = lax.axis_index("frame")
    frames = lax.axis_size("frame")
    channels, row_count, col_count = (features.shape[1], features.shape[2], features.shape[3])
    padded = padded_2(features, (("space", 2),), 1)
    encoded = finish(padded, enc_w, enc_b, row_count, col_count)
    hidden_count = mix_w.shape[0]
    per_group = frames * channels // GROUPS
    group_width = hidden_count // GROUPS
    local_groups = max(1, channels // per_group)
    own_groups = project(encoded[0], mix_w, mix_b, frames, group_width)
    margin = padded_2(own_groups, (("space", 1),), 5)
    margin = jnp.pad(margin, ((0, 0), (0, 0), (5, 5)))
    summed = branches(margin, (branch3, branch5, branch7, branch11), branch_b, row_count, col_count)
    joined = (summed + encoded[0].astype(jnp.float32)).astype(jnp.bfloat16)[None]
    padded_dec = padded_2(joined, (("space", 2),), 1)
    return finish(padded_dec, dec_w, dec_b, row_count, col_count)


def solution(mesh):
    placed = (
        P("frame", None, "space", None),
        P(),
        P(),
        P(),
        P(),
        P(None, None, "frame", None),
        P(None, None, "frame", None),
        P(None, None, "frame", None),
        P(None, None, "frame", None),
        P(None, "frame"),
        P(),
        P(),
    )
    return jax.shard_map(
        per_device,
        mesh=mesh,
        in_specs=placed,
        out_specs=P("frame", None, "space", None),
        check_vma=False,
    )
```

```python
import jax
import jax.numpy as jnp
from jax import lax
from jax.sharding import PartitionSpec as P

GROUPS = 8


def padded_2(block, sides, width):
    for axis, dim in sides:
        count = lax.axis_size(axis)
        forward = [(i, i + 1) for i in range(count - 1)]
        backward = [(target, source) for source, target in forward]
        low = lax.ppermute(
            lax.slice_in_dim(block, block.shape[dim] - width, None, axis=dim), axis, forward
        )
        high = lax.ppermute(lax.slice_in_dim(block, 0, width, axis=dim), axis, backward)
        block = jnp.concatenate([low, block, high], axis=dim)
    return block


def project(encoded, mix_w, mix_b, frames, group_width):
    channels, row_count, col_count = encoded.shape
    rows = row_count // frames
    blocks = encoded.reshape(channels, frames, rows, col_count).transpose(1, 0, 2, 3)
    stacked = lax.all_to_all(blocks, "frame", 0, 0, tiled=False)
    stacked = stacked.reshape(frames * channels, rows, col_count)
    hidden = (
        jnp.einsum("ji,irw->jrw", mix_w, stacked, preferred_element_type=jnp.float32)
        + mix_b[:, None, None]
    ).astype(jnp.bfloat16)
    hidden = hidden.reshape(GROUPS, group_width, rows, col_count)
    hidden = jnp.repeat(hidden, frames // GROUPS, axis=0)
    own = lax.all_to_all(hidden, "frame", 0, 0, tiled=False)
    return own.transpose(1, 0, 2, 3).reshape(group_width, row_count, col_count)


def branches(margin, weights, biases, row_count, col_count):
    half = max(w.shape[0] for w in weights) // 2
    shifted = jnp.stack(
        [lax.slice_in_dim(margin, b, b + col_count, axis=2) for b in range(2 * half + 1)]
    )
    summed = jnp.zeros((weights[0].shape[2], row_count, col_count), jnp.float32)
    for index, weight in enumerate(weights):
        k = weight.shape[0]
        low = half - k // 2
        acc = jnp.zeros_like(summed)
        for a in range(k):
            window = lax.slice_in_dim(shifted, low, low + k, axis=0)
            window = lax.slice_in_dim(window, low + a, low + a + row_count, axis=2)
            acc = acc + jnp.einsum(
                "doi,dirw->orw", weight[a], window, preferred_element_type=jnp.float32
            )
        acc = acc + biases[index][:, None, None]
        summed = summed + jnp.where(acc > 0, acc, 0.2 * acc)
    return summed


def sweep(padded, weight, kernel_size, start, row_count, col_count):
    summed = jnp.zeros((padded.shape[0], weight.shape[3], row_count, col_count), jnp.float32)
    for row_tap in range(kernel_size):
        band = lax.slice_in_dim(padded, start + row_tap, start + row_tap + row_count, axis=2)
        window = jnp.stack(
            [
                lax.slice_in_dim(band, start + col_tap, start + col_tap + col_count, axis=3)
                for col_tap in range(kernel_size)
            ],
            axis=2,
        )
        summed = summed + jnp.einsum(
            "dgoi,gidrw->gorw", weight[row_tap], window, preferred_element_type=jnp.float32
        )
    return summed


def finish(padded, weight, bias, row_count, col_count):
    padded = jnp.pad(padded, ((0, 0), (0, 0), (0, 0), (1, 1)))
    summed = sweep(padded, weight[:, :, None], 3, 0, row_count, col_count)
    return jax.nn.silu(summed + bias[None, :, None, None]).astype(jnp.bfloat16)


def per_device(
    features,
    enc_w,
    enc_b,
    mix_w,
    mix_b,
    branch3,
    branch5,
    branch7,
    branch11,
    branch_b,
    dec_w,
    dec_b,
):
    frame_index = lax.axis_index("frame")
    frames = lax.axis_size("frame")
    channels, row_count, col_count = (features.shape[1], features.shape[2], features.shape[3])
    padded = padded_2(features, (("space", 2),), 2)
    encoded = finish(padded, enc_w, enc_b, row_count + 2, col_count)
    hidden_count = mix_w.shape[0]
    per_group = frames * channels // GROUPS
    group_width = hidden_count // GROUPS
    own_groups = project(encoded[0, :, 1:-1], mix_w, mix_b, frames, group_width)
    margin = padded_2(own_groups, (("space", 1),), 6)
    margin = jnp.pad(margin, ((0, 0), (0, 0), (5, 5)))
    summed = branches(
        margin, (branch3, branch5, branch7, branch11), branch_b, row_count + 2, col_count
    )
    joined = (summed + encoded[0].astype(jnp.float32)).astype(jnp.bfloat16)
    strip = lax.axis_index("space")
    rows = lax.broadcasted_iota(jnp.int32, (1, row_count + 2, 1), 1)
    inside = ((rows > 0) | (strip > 0)) & ((rows < row_count + 1) | (strip < lax.axis_size("space") - 1))
    padded_dec = jnp.where(inside, joined, jnp.zeros_like(joined))[None]
    return finish(padded_dec, dec_w, dec_b, row_count, col_count)


def solution(mesh):
    placed = (
        P("frame", None, "space", None),
        P(),
        P(),
        P(),
        P(),
        P(None, None, "frame", None),
        P(None, None, "frame", None),
        P(None, None, "frame", None),
        P(None, None, "frame", None),
        P(None, "frame"),
        P(),
        P(),
    )
    return jax.shard_map(
        per_device,
        mesh=mesh,
        in_specs=placed,
        out_specs=P("frame", None, "space", None),
        check_vma=False,
    )
```

```python
import jax
import jax.numpy as jnp
from jax import lax
from jax.sharding import PartitionSpec as P

GROUPS = 8


def padded_2(block, sides, width):
    for axis, dim in sides:
        count = lax.axis_size(axis)
        forward = [(i, i + 1) for i in range(count - 1)]
        backward = [(target, source) for source, target in forward]
        low = lax.ppermute(
            lax.slice_in_dim(block, block.shape[dim] - width, None, axis=dim), axis, forward
        )
        high = lax.ppermute(lax.slice_in_dim(block, 0, width, axis=dim), axis, backward)
        block = jnp.concatenate([low, block, high], axis=dim)
    return block


def project(encoded, mix_w, mix_b, frames, group_width):
    channels, row_count, col_count = encoded.shape
    rows = row_count // frames
    blocks = encoded.reshape(channels, frames, rows, col_count).transpose(1, 0, 2, 3)
    stacked = lax.all_to_all(blocks, "frame", 0, 0, tiled=False)
    stacked = stacked.reshape(frames * channels, rows, col_count)
    hidden = (
        jnp.einsum("ji,irw->jrw", mix_w, stacked, preferred_element_type=jnp.float32)
        + mix_b[:, None, None]
    ).astype(jnp.bfloat16)
    hidden = hidden.reshape(GROUPS, group_width, rows, col_count)
    hidden = jnp.repeat(hidden, frames // GROUPS, axis=0)
    own = lax.all_to_all(hidden, "frame", 0, 0, tiled=False)
    return own.transpose(1, 0, 2, 3).reshape(group_width, row_count, col_count)


def branches(margin, weights, biases, row_count, col_count):
    half = max(w.shape[0] for w in weights) // 2
    shifted = jnp.stack(
        [lax.slice_in_dim(margin, b, b + col_count, axis=2) for b in range(2 * half + 1)]
    )
    summed = jnp.zeros((weights[0].shape[2], row_count, col_count), jnp.float32)
    for index, weight in enumerate(weights):
        k = weight.shape[0]
        low = half - k // 2
        acc = jnp.zeros_like(summed)
        for a in range(k):
            window = lax.slice_in_dim(shifted, low, low + k, axis=0)
            window = lax.slice_in_dim(window, low + a, low + a + row_count, axis=2)
            acc = acc + jnp.einsum(
                "doi,dirw->orw", weight[a], window, preferred_element_type=jnp.float32
            )
        acc = acc + biases[index][:, None, None]
        summed = summed + jnp.where(acc > 0, acc, 0.2 * acc)
    return summed


def sweep(padded, weight, kernel_size, start, row_count, col_count):
    summed = jnp.zeros((padded.shape[0], weight.shape[3], row_count, col_count), jnp.float32)
    for row_tap in range(kernel_size):
        band = lax.slice_in_dim(padded, start + row_tap, start + row_tap + row_count, axis=2)
        window = jnp.stack(
            [
                lax.slice_in_dim(band, start + col_tap, start + col_tap + col_count, axis=3)
                for col_tap in range(kernel_size)
            ],
            axis=2,
        )
        summed = summed + jnp.einsum(
            "dgoi,gidrw->gorw", weight[row_tap], window, preferred_element_type=jnp.float32
        )
    return summed


def finish(padded, weight, bias, row_count, col_count):
    padded = jnp.pad(padded[0], ((0, 0), (0, 0), (1, 1)))
    shifted = jnp.stack(
        [lax.slice_in_dim(padded, b, b + col_count, axis=2) for b in range(weight.shape[1])]
    )
    summed = jnp.zeros((weight.shape[2], row_count, col_count), jnp.float32)
    for a in range(weight.shape[0]):
        window = lax.slice_in_dim(shifted, a, a + row_count, axis=2)
        summed = summed + jnp.einsum(
            "doi,dirw->orw", weight[a], window, preferred_element_type=jnp.float32
        )
    return jax.nn.silu(summed + bias[:, None, None]).astype(jnp.bfloat16)[None]


def per_device(
    features,
    enc_w,
    enc_b,
    mix_w,
    mix_b,
    branch3,
    branch5,
    branch7,
    branch11,
    branch_b,
    dec_w,
    dec_b,
):
    frame_index = lax.axis_index("frame")
    frames = lax.axis_size("frame")
    channels, row_count, col_count = (features.shape[1], features.shape[2], features.shape[3])
    padded = padded_2(features, (("space", 2),), 2)
    encoded = finish(padded, enc_w, enc_b, row_count + 2, col_count)
    hidden_count = mix_w.shape[0]
    per_group = frames * channels // GROUPS
    group_width = hidden_count // GROUPS
    own_groups = project(encoded[0, :, 1:-1], mix_w, mix_b, frames, group_width)
    margin = padded_2(own_groups, (("space", 1),), 6)
    margin = jnp.pad(margin, ((0, 0), (0, 0), (5, 5)))
    summed = branches(
        margin, (branch3, branch5, branch7, branch11), branch_b, row_count + 2, col_count
    )
    joined = (summed + encoded[0].astype(jnp.float32)).astype(jnp.bfloat16)
    strip = lax.axis_index("space")
    rows = lax.broadcasted_iota(jnp.int32, (1, row_count + 2, 1), 1)
    inside = ((rows > 0) | (strip > 0)) & ((rows < row_count + 1) | (strip < lax.axis_size("space") - 1))
    padded_dec = jnp.where(inside, joined, jnp.zeros_like(joined))[None]
    return finish(padded_dec, dec_w, dec_b, row_count, col_count)


def solution(mesh):
    placed = (
        P("frame", None, "space", None),
        P(),
        P(),
        P(),
        P(),
        P(None, None, "frame", None),
        P(None, None, "frame", None),
        P(None, None, "frame", None),
        P(None, None, "frame", None),
        P(None, "frame"),
        P(),
        P(),
    )
    return jax.shard_map(
        per_device,
        mesh=mesh,
        in_specs=placed,
        out_specs=P("frame", None, "space", None),
        check_vma=False,
    )
```

```python
import jax
import jax.numpy as jnp
from jax import lax
from jax.sharding import PartitionSpec as P

GROUPS = 8


def halo_rows(block, axis, dim, width):
    count = lax.axis_size(axis)
    forward = [(i, i + 1) for i in range(count - 1)]
    backward = [(target, source) for source, target in forward]
    low = lax.ppermute(
        lax.slice_in_dim(block, block.shape[dim] - width, None, axis=dim), axis, forward
    )
    high = lax.ppermute(lax.slice_in_dim(block, 0, width, axis=dim), axis, backward)
    return low, high


def padded_2(block, sides, width):
    for axis, dim in sides:
        count = lax.axis_size(axis)
        forward = [(i, i + 1) for i in range(count - 1)]
        backward = [(target, source) for source, target in forward]
        low = lax.ppermute(
            lax.slice_in_dim(block, block.shape[dim] - width, None, axis=dim), axis, forward
        )
        high = lax.ppermute(lax.slice_in_dim(block, 0, width, axis=dim), axis, backward)
        block = jnp.concatenate([low, block, high], axis=dim)
    return block


def project(encoded, mix_w, mix_b, frames, group_width):
    channels, row_count, col_count = encoded.shape
    rows = row_count // frames
    blocks = encoded.reshape(channels, frames, rows, col_count).transpose(1, 0, 2, 3)
    stacked = lax.all_to_all(blocks, "frame", 0, 0, tiled=False)
    stacked = stacked.reshape(frames * channels, rows, col_count)
    hidden = (
        jnp.einsum("ji,irw->jrw", mix_w, stacked, preferred_element_type=jnp.float32)
        + mix_b[:, None, None]
    ).astype(jnp.bfloat16)
    hidden = hidden.reshape(GROUPS, group_width, rows, col_count)
    hidden = jnp.repeat(hidden, frames // GROUPS, axis=0)
    own = lax.all_to_all(hidden, "frame", 0, 0, tiled=False)
    return own.transpose(1, 0, 2, 3).reshape(group_width, row_count, col_count)


def branches(margin, weights, biases, row_count, col_count):
    half = max(w.shape[0] for w in weights) // 2
    shifted = jnp.stack(
        [lax.slice_in_dim(margin, b, b + col_count, axis=2) for b in range(2 * half + 1)]
    )
    summed = jnp.zeros((weights[0].shape[2], row_count, col_count), jnp.float32)
    for index, weight in enumerate(weights):
        k = weight.shape[0]
        low = half - k // 2
        acc = jnp.zeros_like(summed)
        for a in range(k):
            window = lax.slice_in_dim(shifted, low, low + k, axis=0)
            window = lax.slice_in_dim(window, low + a, low + a + row_count, axis=2)
            acc = acc + jnp.einsum(
                "doi,dirw->orw", weight[a], window, preferred_element_type=jnp.float32
            )
        acc = acc + biases[index][:, None, None]
        summed = summed + jnp.where(acc > 0, acc, 0.2 * acc)
    return summed


def sweep(padded, weight, kernel_size, start, row_count, col_count):
    summed = jnp.zeros((padded.shape[0], weight.shape[3], row_count, col_count), jnp.float32)
    for row_tap in range(kernel_size):
        band = lax.slice_in_dim(padded, start + row_tap, start + row_tap + row_count, axis=2)
        window = jnp.stack(
            [
                lax.slice_in_dim(band, start + col_tap, start + col_tap + col_count, axis=3)
                for col_tap in range(kernel_size)
            ],
            axis=2,
        )
        summed = summed + jnp.einsum(
            "dgoi,gidrw->gorw", weight[row_tap], window, preferred_element_type=jnp.float32
        )
    return summed


def finish(padded, weight, bias, row_count, col_count):
    padded = jnp.pad(padded[0], ((0, 0), (0, 0), (1, 1)))
    shifted = jnp.stack(
        [lax.slice_in_dim(padded, b, b + col_count, axis=2) for b in range(weight.shape[1])]
    )
    summed = jnp.zeros((weight.shape[2], row_count, col_count), jnp.float32)
    for a in range(weight.shape[0]):
        window = lax.slice_in_dim(shifted, a, a + row_count, axis=2)
        summed = summed + jnp.einsum(
            "doi,dirw->orw", weight[a], window, preferred_element_type=jnp.float32
        )
    return jax.nn.silu(summed + bias[:, None, None]).astype(jnp.bfloat16)[None]


def per_device(
    features,
    enc_w,
    enc_b,
    mix_w,
    mix_b,
    branch3,
    branch5,
    branch7,
    branch11,
    branch_b,
    dec_w,
    dec_b,
):
    frame_index = lax.axis_index("frame")
    frames = lax.axis_size("frame")
    channels, row_count, col_count = (features.shape[1], features.shape[2], features.shape[3])
    low, high = halo_rows(features, "space", 2, 2)
    encoded = jnp.concatenate(
        [
            finish(jnp.concatenate([low, features[:, :, :2]], axis=2), enc_w, enc_b, 2, col_count),
            finish(features, enc_w, enc_b, row_count - 2, col_count),
            finish(jnp.concatenate([features[:, :, -2:], high], axis=2), enc_w, enc_b, 2, col_count),
        ],
        axis=2,
    )
    hidden_count = mix_w.shape[0]
    per_group = frames * channels // GROUPS
    group_width = hidden_count // GROUPS
    own_groups = project(encoded[0, :, 1:-1], mix_w, mix_b, frames, group_width)
    margin = padded_2(own_groups, (("space", 1),), 6)
    margin = jnp.pad(margin, ((0, 0), (0, 0), (5, 5)))
    summed = branches(
        margin, (branch3, branch5, branch7, branch11), branch_b, row_count + 2, col_count
    )
    joined = (summed + encoded[0].astype(jnp.float32)).astype(jnp.bfloat16)
    strip = lax.axis_index("space")
    rows = lax.broadcasted_iota(jnp.int32, (1, row_count + 2, 1), 1)
    inside = ((rows > 0) | (strip > 0)) & ((rows < row_count + 1) | (strip < lax.axis_size("space") - 1))
    padded_dec = jnp.where(inside, joined, jnp.zeros_like(joined))[None]
    return finish(padded_dec, dec_w, dec_b, row_count, col_count)


def solution(mesh):
    placed = (
        P("frame", None, "space", None),
        P(),
        P(),
        P(),
        P(),
        P(None, None, "frame", None),
        P(None, None, "frame", None),
        P(None, None, "frame", None),
        P(None, None, "frame", None),
        P(None, "frame"),
        P(),
        P(),
    )
    return jax.shard_map(
        per_device,
        mesh=mesh,
        in_specs=placed,
        out_specs=P("frame", None, "space", None),
        check_vma=False,
    )
```

```python
import jax
import jax.numpy as jnp
from jax import lax
from jax.sharding import PartitionSpec as P


GROUPS = 8


def halo_rows(block, axis, dim, width):
    count = lax.axis_size(axis)
    forward = [(i, i + 1) for i in range(count - 1)]
    backward = [(target, source) for source, target in forward]
    low = lax.ppermute(
        lax.slice_in_dim(block, block.shape[dim] - width, None, axis=dim), axis, forward
    )
    high = lax.ppermute(lax.slice_in_dim(block, 0, width, axis=dim), axis, backward)
    return low, high


def project(encoded, mix_w, mix_b, frames, group_width):
    channels, row_count, col_count = encoded.shape
    rows = row_count // frames
    blocks = encoded.reshape(channels, frames, rows, col_count).transpose(1, 0, 2, 3)
    stacked = lax.all_to_all(blocks, "frame", 0, 0, tiled=False)
    stacked = stacked.reshape(frames * channels, rows, col_count)
    hidden = (
        jnp.einsum("ji,irw->jrw", mix_w, stacked, preferred_element_type=jnp.float32)
        + mix_b[:, None, None]
    ).astype(jnp.bfloat16)
    hidden = hidden.reshape(GROUPS, group_width, rows, col_count)
    hidden = jnp.repeat(hidden, frames // GROUPS, axis=0)
    own = lax.all_to_all(hidden, "frame", 0, 0, tiled=False)
    return own.transpose(1, 0, 2, 3).reshape(group_width, row_count, col_count)


def branches(margin, weights, biases, row_count, col_count):
    half = max(w.shape[0] for w in weights) // 2
    shifted = jnp.stack(
        [lax.slice_in_dim(margin, b, b + col_count, axis=2) for b in range(2 * half + 1)]
    )
    summed = jnp.zeros((weights[0].shape[2], row_count, col_count), jnp.float32)
    for index, weight in enumerate(weights):
        k = weight.shape[0]
        low = half - k // 2
        acc = jnp.zeros_like(summed)
        for a in range(k):
            window = lax.slice_in_dim(shifted, low, low + k, axis=0)
            window = lax.slice_in_dim(window, low + a, low + a + row_count, axis=2)
            acc = acc + jnp.einsum(
                "doi,dirw->orw", weight[a], window, preferred_element_type=jnp.float32
            )
        acc = acc + biases[index][:, None, None]
        summed = summed + jnp.where(acc > 0, acc, 0.2 * acc)
    return summed


def finish(padded, weight, bias, row_count, col_count):
    padded = jnp.pad(padded[0], ((0, 0), (0, 0), (1, 1)))
    shifted = jnp.stack(
        [lax.slice_in_dim(padded, b, b + col_count, axis=2) for b in range(weight.shape[1])]
    )
    summed = jnp.zeros((weight.shape[2], row_count, col_count), jnp.float32)
    for a in range(weight.shape[0]):
        window = lax.slice_in_dim(shifted, a, a + row_count, axis=2)
        summed = summed + jnp.einsum(
            "doi,dirw->orw", weight[a], window, preferred_element_type=jnp.float32
        )
    return jax.nn.silu(summed + bias[:, None, None]).astype(jnp.bfloat16)[None]


def per_device(
    features,
    enc_w,
    enc_b,
    mix_w,
    mix_b,
    branch3,
    branch5,
    branch7,
    branch11,
    branch_b,
    dec_w,
    dec_b,
):
    frames = lax.axis_size("frame")
    row_count, col_count = (features.shape[2], features.shape[3])
    low, high = halo_rows(features, "space", 2, 2)
    encoded = jnp.concatenate(
        [
            finish(jnp.concatenate([low, features[:, :, :2]], axis=2), enc_w, enc_b, 2, col_count),
            finish(features, enc_w, enc_b, row_count - 2, col_count),
            finish(jnp.concatenate([features[:, :, -2:], high], axis=2), enc_w, enc_b, 2, col_count),
        ],
        axis=2,
    )
    hidden_count = mix_w.shape[0]
    group_width = hidden_count // GROUPS
    own_groups = project(encoded[0, :, 1:-1], mix_w, mix_b, frames, group_width)
    kernels = (branch3, branch5, branch7, branch11)
    reach = 6
    low, high = halo_rows(own_groups, "space", 1, reach)
    middle = branches(
        jnp.pad(own_groups, ((0, 0), (0, 0), (5, 5))),
        kernels,
        branch_b,
        row_count - 2 * (reach - 1),
        col_count,
    )
    top = jnp.concatenate([low, own_groups[:, : 2 * reach - 2]], axis=1)
    bottom = jnp.concatenate([own_groups[:, row_count - 2 * reach + 2 :], high], axis=1)
    side = jnp.pad(
        jnp.concatenate([top, jnp.zeros_like(top[:, :, :10]), bottom], axis=2),
        ((0, 0), (0, 0), (5, 5)),
    )
    edges = branches(side, kernels, branch_b, reach, 2 * col_count + 10)
    summed = jnp.concatenate(
        [edges[:, :, :col_count], middle, edges[:, :, col_count + 10 :]], axis=1
    )
    joined = (summed + encoded[0].astype(jnp.float32)).astype(jnp.bfloat16)
    strip = lax.axis_index("space")
    rows = lax.broadcasted_iota(jnp.int32, (1, row_count + 2, 1), 1)
    inside = ((rows > 0) | (strip > 0)) & ((rows < row_count + 1) | (strip < lax.axis_size("space") - 1))
    padded_dec = jnp.where(inside, joined, jnp.zeros_like(joined))[None]
    return finish(padded_dec, dec_w, dec_b, row_count, col_count)


def solution(mesh):
    placed = (
        P("frame", None, "space", None),
        P(),
        P(),
        P(),
        P(),
        P(None, None, "frame", None),
        P(None, None, "frame", None),
        P(None, None, "frame", None),
        P(None, None, "frame", None),
        P(None, "frame"),
        P(),
        P(),
    )

    return jax.shard_map(
        per_device,
        mesh=mesh,
        in_specs=placed,
        out_specs=P("frame", None, "space", None),
        check_vma=False,
    )
```

```python
import jax
import jax.numpy as jnp
from jax import lax
from jax.sharding import PartitionSpec as P

GROUPS = 8


def halo_rows(block, axis, dim, width):
    count = lax.axis_size(axis)
    forward = [(i, i + 1) for i in range(count - 1)]
    backward = [(target, source) for source, target in forward]
    low = lax.ppermute(
        lax.slice_in_dim(block, block.shape[dim] - width, None, axis=dim), axis, forward
    )
    high = lax.ppermute(lax.slice_in_dim(block, 0, width, axis=dim), axis, backward)
    return low, high


def padded_2(block, sides, width):
    for axis, dim in sides:
        count = lax.axis_size(axis)
        forward = [(i, i + 1) for i in range(count - 1)]
        backward = [(target, source) for source, target in forward]
        low = lax.ppermute(
            lax.slice_in_dim(block, block.shape[dim] - width, None, axis=dim), axis, forward
        )
        high = lax.ppermute(lax.slice_in_dim(block, 0, width, axis=dim), axis, backward)
        block = jnp.concatenate([low, block, high], axis=dim)
    return block


def project(encoded, mix_w, mix_b, frames, group_width):
    channels, row_count, col_count = encoded.shape
    stacked = lax.all_to_all(encoded, "frame", 1, 0, tiled=True)
    hidden = (
        jnp.einsum("ji,irw->jrw", mix_w, stacked, preferred_element_type=jnp.float32)
        + mix_b[:, None, None]
    ).astype(jnp.bfloat16)
    rows = hidden.shape[1]
    hidden = hidden.reshape(GROUPS, group_width, rows, col_count)
    hidden = jnp.repeat(hidden, frames // GROUPS, axis=0)
    hidden = hidden.reshape(frames * group_width, rows, col_count)
    return lax.all_to_all(hidden, "frame", 0, 1, tiled=True)


def branches(margin, weights, biases, row_count, col_count):
    half = max(w.shape[0] for w in weights) // 2
    shifted = jnp.stack(
        [lax.slice_in_dim(margin, b, b + col_count, axis=2) for b in range(2 * half + 1)]
    )
    summed = jnp.zeros((weights[0].shape[2], row_count, col_count), jnp.float32)
    for index, weight in enumerate(weights):
        k = weight.shape[0]
        low = half - k // 2
        acc = jnp.zeros_like(summed)
        for a in range(k):
            window = lax.slice_in_dim(shifted, low, low + k, axis=0)
            window = lax.slice_in_dim(window, low + a, low + a + row_count, axis=2)
            acc = acc + jnp.einsum(
                "doi,dirw->orw", weight[a], window, preferred_element_type=jnp.float32
            )
        acc = acc + biases[index][:, None, None]
        summed = summed + jnp.where(acc > 0, acc, 0.2 * acc)
    return summed


def sweep(padded, weight, kernel_size, start, row_count, col_count):
    summed = jnp.zeros((padded.shape[0], weight.shape[3], row_count, col_count), jnp.float32)
    for row_tap in range(kernel_size):
        band = lax.slice_in_dim(padded, start + row_tap, start + row_tap + row_count, axis=2)
        window = jnp.stack(
            [
                lax.slice_in_dim(band, start + col_tap, start + col_tap + col_count, axis=3)
                for col_tap in range(kernel_size)
            ],
            axis=2,
        )
        summed = summed + jnp.einsum(
            "dgoi,gidrw->gorw", weight[row_tap], window, preferred_element_type=jnp.float32
        )
    return summed


def finish(padded, weight, bias, row_count, col_count):
    padded = jnp.pad(padded[0], ((0, 0), (0, 0), (1, 1)))
    shifted = jnp.stack(
        [lax.slice_in_dim(padded, b, b + col_count, axis=2) for b in range(weight.shape[1])]
    )
    summed = jnp.zeros((weight.shape[2], row_count, col_count), jnp.float32)
    for a in range(weight.shape[0]):
        window = lax.slice_in_dim(shifted, a, a + row_count, axis=2)
        summed = summed + jnp.einsum(
            "doi,dirw->orw", weight[a], window, preferred_element_type=jnp.float32
        )
    return jax.nn.silu(summed + bias[:, None, None]).astype(jnp.bfloat16)[None]


def per_device(
    features,
    enc_w,
    enc_b,
    mix_w,
    mix_b,
    branch3,
    branch5,
    branch7,
    branch11,
    branch_b,
    dec_w,
    dec_b,
):
    frame_index = lax.axis_index("frame")
    frames = lax.axis_size("frame")
    channels, row_count, col_count = (features.shape[1], features.shape[2], features.shape[3])
    low, high = halo_rows(features, "space", 2, 2)
    encoded = jnp.concatenate(
        [
            finish(jnp.concatenate([low, features[:, :, :2]], axis=2), enc_w, enc_b, 2, col_count),
            finish(features, enc_w, enc_b, row_count - 2, col_count),
            finish(jnp.concatenate([features[:, :, -2:], high], axis=2), enc_w, enc_b, 2, col_count),
        ],
        axis=2,
    )
    hidden_count = mix_w.shape[0]
    per_group = frames * channels // GROUPS
    group_width = hidden_count // GROUPS
    own_groups = project(encoded[0, :, 1:-1], mix_w, mix_b, frames, group_width)
    margin = padded_2(own_groups, (("space", 1),), 6)
    margin = jnp.pad(margin, ((0, 0), (0, 0), (5, 5)))
    summed = branches(
        margin, (branch3, branch5, branch7, branch11), branch_b, row_count + 2, col_count
    )
    joined = (summed + encoded[0].astype(jnp.float32)).astype(jnp.bfloat16)
    strip = lax.axis_index("space")
    rows = lax.broadcasted_iota(jnp.int32, (1, row_count + 2, 1), 1)
    inside = ((rows > 0) | (strip > 0)) & ((rows < row_count + 1) | (strip < lax.axis_size("space") - 1))
    padded_dec = jnp.where(inside, joined, jnp.zeros_like(joined))[None]
    return finish(padded_dec, dec_w, dec_b, row_count, col_count)


def solution(mesh):
    placed = (
        P("frame", None, "space", None),
        P(),
        P(),
        P(),
        P(),
        P(None, None, "frame", None),
        P(None, None, "frame", None),
        P(None, None, "frame", None),
        P(None, None, "frame", None),
        P(None, "frame"),
        P(),
        P(),
    )
    return jax.shard_map(
        per_device,
        mesh=mesh,
        in_specs=placed,
        out_specs=P("frame", None, "space", None),
        check_vma=False,
    )
```

```python
import jax
import jax.numpy as jnp
from jax import lax
from jax.sharding import PartitionSpec as P

GROUPS = 8


def halo_rows(block, axis, dim, width):
    count = lax.axis_size(axis)
    forward = [(i, i + 1) for i in range(count - 1)]
    backward = [(target, source) for source, target in forward]
    low = lax.ppermute(
        lax.slice_in_dim(block, block.shape[dim] - width, None, axis=dim), axis, forward
    )
    high = lax.ppermute(lax.slice_in_dim(block, 0, width, axis=dim), axis, backward)
    return low, high


def padded_2(block, sides, width):
    for axis, dim in sides:
        count = lax.axis_size(axis)
        forward = [(i, i + 1) for i in range(count - 1)]
        backward = [(target, source) for source, target in forward]
        low = lax.ppermute(
            lax.slice_in_dim(block, block.shape[dim] - width, None, axis=dim), axis, forward
        )
        high = lax.ppermute(lax.slice_in_dim(block, 0, width, axis=dim), axis, backward)
        block = jnp.concatenate([low, block, high], axis=dim)
    return block


def project(encoded, mix_w, mix_b, frames, group_width):
    channels, row_count, col_count = encoded.shape
    rows = row_count // frames
    blocks = encoded.reshape(channels, frames, rows, col_count).transpose(1, 0, 2, 3)
    stacked = lax.all_to_all(blocks, "frame", 0, 0, tiled=False)
    stacked = stacked.reshape(frames * channels, rows, col_count)
    hidden = (
        jnp.einsum("ji,irw->jrw", mix_w, stacked, preferred_element_type=jnp.float32)
        + mix_b[:, None, None]
    ).astype(jnp.bfloat16)
    hidden = hidden.reshape(GROUPS, group_width, rows, col_count)
    hidden = jnp.repeat(hidden, frames // GROUPS, axis=0)
    own = lax.all_to_all(hidden, "frame", 0, 0, tiled=False)
    return own.transpose(1, 0, 2, 3).reshape(group_width, row_count, col_count)


def branches(margin, weights, biases, row_count, col_count):
    half = max(w.shape[0] for w in weights) // 2
    shifted = jnp.stack(
        [lax.slice_in_dim(margin, b, b + col_count, axis=2) for b in range(2 * half + 1)]
    )
    summed = jnp.zeros((weights[0].shape[2], row_count, col_count), jnp.float32)
    for index, weight in enumerate(weights):
        k = weight.shape[0]
        low = half - k // 2
        acc = jnp.zeros_like(summed)
        for a in range(k):
            window = lax.slice_in_dim(shifted, low, low + k, axis=0)
            window = lax.slice_in_dim(window, low + a, low + a + row_count, axis=2)
            acc = acc + jnp.einsum(
                "doi,dirw->orw", weight[a], window, preferred_element_type=jnp.float32
            )
        acc = acc + biases[index][:, None, None]
        summed = summed + jnp.where(acc > 0, acc, 0.2 * acc)
    return summed


def sweep(padded, weight, kernel_size, start, row_count, col_count):
    summed = jnp.zeros((padded.shape[0], weight.shape[3], row_count, col_count), jnp.float32)
    for row_tap in range(kernel_size):
        band = lax.slice_in_dim(padded, start + row_tap, start + row_tap + row_count, axis=2)
        window = jnp.stack(
            [
                lax.slice_in_dim(band, start + col_tap, start + col_tap + col_count, axis=3)
                for col_tap in range(kernel_size)
            ],
            axis=2,
        )
        summed = summed + jnp.einsum(
            "dgoi,gidrw->gorw", weight[row_tap], window, preferred_element_type=jnp.float32
        )
    return summed


def finish(padded, weight, bias, row_count, col_count):
    padded = jnp.pad(padded[0], ((0, 0), (0, 0), (1, 1)))
    shifted = jnp.stack(
        [lax.slice_in_dim(padded, b, b + col_count, axis=2) for b in range(weight.shape[1])]
    )
    summed = jnp.zeros((weight.shape[2], row_count, col_count), jnp.float32)
    for a in range(weight.shape[0]):
        window = lax.slice_in_dim(shifted, a, a + row_count, axis=2)
        summed = summed + jnp.einsum(
            "doi,dirw->orw", weight[a], window, preferred_element_type=jnp.float32
        )
    return jax.nn.silu(summed + bias[:, None, None]).astype(jnp.bfloat16)[None]


def per_device(
    features,
    enc_w,
    enc_b,
    mix_w,
    mix_b,
    branch3,
    branch5,
    branch7,
    branch11,
    branch_b,
    dec_w,
    dec_b,
):
    frame_index = lax.axis_index("frame")
    frames = lax.axis_size("frame")
    channels, row_count, col_count = (features.shape[1], features.shape[2], features.shape[3])
    low, high = halo_rows(features, "space", 2, 2)
    above = jnp.concatenate([low, features[:, :, :2]], axis=2)
    below = jnp.concatenate([features[:, :, -2:], high], axis=2)
    inner = jnp.concatenate(
        [
            finish(above[:, :, 1:], enc_w, enc_b, 1, col_count),
            finish(features, enc_w, enc_b, row_count - 2, col_count),
            finish(below[:, :, :-1], enc_w, enc_b, 1, col_count),
        ],
        axis=2,
    )
    encoded = jnp.concatenate(
        [
            finish(above[:, :, :-1], enc_w, enc_b, 1, col_count),
            inner,
            finish(below[:, :, 1:], enc_w, enc_b, 1, col_count),
        ],
        axis=2,
    )
    hidden_count = mix_w.shape[0]
    per_group = frames * channels // GROUPS
    group_width = hidden_count // GROUPS
    own_groups = project(inner[0], mix_w, mix_b, frames, group_width)
    margin = padded_2(own_groups, (("space", 1),), 6)
    margin = jnp.pad(margin, ((0, 0), (0, 0), (5, 5)))
    summed = branches(
        margin, (branch3, branch5, branch7, branch11), branch_b, row_count + 2, col_count
    )
    joined = (summed + encoded[0].astype(jnp.float32)).astype(jnp.bfloat16)
    strip = lax.axis_index("space")
    rows = lax.broadcasted_iota(jnp.int32, (1, row_count + 2, 1), 1)
    inside = ((rows > 0) | (strip > 0)) & ((rows < row_count + 1) | (strip < lax.axis_size("space") - 1))
    padded_dec = jnp.where(inside, joined, jnp.zeros_like(joined))[None]
    return finish(padded_dec, dec_w, dec_b, row_count, col_count)


def solution(mesh):
    placed = (
        P("frame", None, "space", None),
        P(),
        P(),
        P(),
        P(),
        P(None, None, "frame", None),
        P(None, None, "frame", None),
        P(None, None, "frame", None),
        P(None, None, "frame", None),
        P(None, "frame"),
        P(),
        P(),
    )
    return jax.shard_map(
        per_device,
        mesh=mesh,
        in_specs=placed,
        out_specs=P("frame", None, "space", None),
        check_vma=False,
    )
```

```python
import jax
import jax.numpy as jnp
from jax import lax
from jax.sharding import PartitionSpec as P

GROUPS = 8


def halo_rows(block, axis, dim, width):
    count = lax.axis_size(axis)
    forward = [(i, i + 1) for i in range(count - 1)]
    backward = [(target, source) for source, target in forward]
    low = lax.ppermute(
        lax.slice_in_dim(block, block.shape[dim] - width, None, axis=dim), axis, forward
    )
    high = lax.ppermute(lax.slice_in_dim(block, 0, width, axis=dim), axis, backward)
    return low, high


def padded_2(block, sides, width):
    for axis, dim in sides:
        count = lax.axis_size(axis)
        forward = [(i, i + 1) for i in range(count - 1)]
        backward = [(target, source) for source, target in forward]
        low = lax.ppermute(
            lax.slice_in_dim(block, block.shape[dim] - width, None, axis=dim), axis, forward
        )
        high = lax.ppermute(lax.slice_in_dim(block, 0, width, axis=dim), axis, backward)
        block = jnp.concatenate([low, block, high], axis=dim)
    return block


def project(encoded, mix_w, mix_b, frames, group_width):
    channels, row_count, col_count = encoded.shape
    rows = row_count // frames
    blocks = encoded.reshape(channels, frames, rows, col_count).transpose(1, 0, 2, 3)
    stacked = lax.all_to_all(blocks, "frame", 0, 0, tiled=False)
    stacked = stacked.reshape(frames * channels, rows, col_count)
    hidden = (
        jnp.einsum("ji,irw->jrw", mix_w, stacked, preferred_element_type=jnp.float32)
        + mix_b[:, None, None]
    ).astype(jnp.bfloat16)
    hidden = hidden.reshape(GROUPS, group_width, rows, col_count)
    hidden = jnp.repeat(hidden, frames // GROUPS, axis=0)
    own = lax.all_to_all(hidden, "frame", 0, 0, tiled=False)
    return own.transpose(1, 0, 2, 3).reshape(group_width, row_count, col_count)


def branches(margin, weights, biases, row_count, col_count):
    half = max(w.shape[0] for w in weights) // 2
    shifted = jnp.stack(
        [lax.slice_in_dim(margin, b, b + col_count, axis=2) for b in range(2 * half + 1)]
    )
    summed = jnp.zeros((weights[0].shape[2], row_count, col_count), jnp.float32)
    for index, weight in enumerate(weights):
        k = weight.shape[0]
        low = half - k // 2
        acc = jnp.zeros_like(summed)
        for a in range(k):
            window = lax.slice_in_dim(shifted, low, low + k, axis=0)
            window = lax.slice_in_dim(window, low + a, low + a + row_count, axis=2)
            acc = acc + jnp.einsum(
                "doi,dirw->orw", weight[a], window, preferred_element_type=jnp.float32
            )
        acc = acc + biases[index][:, None, None]
        summed = summed + jnp.where(acc > 0, acc, 0.2 * acc)
    return summed


def sweep(padded, weight, kernel_size, start, row_count, col_count):
    summed = jnp.zeros((padded.shape[0], weight.shape[3], row_count, col_count), jnp.float32)
    for row_tap in range(kernel_size):
        band = lax.slice_in_dim(padded, start + row_tap, start + row_tap + row_count, axis=2)
        window = jnp.stack(
            [
                lax.slice_in_dim(band, start + col_tap, start + col_tap + col_count, axis=3)
                for col_tap in range(kernel_size)
            ],
            axis=2,
        )
        summed = summed + jnp.einsum(
            "dgoi,gidrw->gorw", weight[row_tap], window, preferred_element_type=jnp.float32
        )
    return summed


def finish(padded, weight, bias, row_count, col_count):
    padded = jnp.pad(padded[0], ((0, 0), (0, 0), (1, 1)))
    shifted = jnp.stack(
        [lax.slice_in_dim(padded, b, b + col_count, axis=2) for b in range(weight.shape[1])]
    )
    summed = jnp.zeros((weight.shape[2], row_count * col_count), jnp.float32)
    for a in range(weight.shape[0]):
        window = lax.slice_in_dim(shifted, a, a + row_count, axis=2)
        window = window.reshape(window.shape[0], window.shape[1], row_count * col_count)
        summed = summed + jnp.einsum(
            "doi,dip->op", weight[a], window, preferred_element_type=jnp.float32
        )
    summed = summed.reshape(weight.shape[2], row_count, col_count)
    return jax.nn.silu(summed + bias[:, None, None]).astype(jnp.bfloat16)[None]


def per_device(
    features,
    enc_w,
    enc_b,
    mix_w,
    mix_b,
    branch3,
    branch5,
    branch7,
    branch11,
    branch_b,
    dec_w,
    dec_b,
):
    frame_index = lax.axis_index("frame")
    frames = lax.axis_size("frame")
    channels, row_count, col_count = (features.shape[1], features.shape[2], features.shape[3])
    low, high = halo_rows(features, "space", 2, 2)
    encoded = jnp.concatenate(
        [
            finish(jnp.concatenate([low, features[:, :, :2]], axis=2), enc_w, enc_b, 2, col_count),
            finish(features, enc_w, enc_b, row_count - 2, col_count),
            finish(jnp.concatenate([features[:, :, -2:], high], axis=2), enc_w, enc_b, 2, col_count),
        ],
        axis=2,
    )
    hidden_count = mix_w.shape[0]
    per_group = frames * channels // GROUPS
    group_width = hidden_count // GROUPS
    own_groups = project(encoded[0, :, 1:-1], mix_w, mix_b, frames, group_width)
    margin = padded_2(own_groups, (("space", 1),), 6)
    margin = jnp.pad(margin, ((0, 0), (0, 0), (5, 5)))
    summed = branches(
        margin, (branch3, branch5, branch7, branch11), branch_b, row_count + 2, col_count
    )
    joined = (summed + encoded[0].astype(jnp.float32)).astype(jnp.bfloat16)
    strip = lax.axis_index("space")
    rows = lax.broadcasted_iota(jnp.int32, (1, row_count + 2, 1), 1)
    inside = ((rows > 0) | (strip > 0)) & ((rows < row_count + 1) | (strip < lax.axis_size("space") - 1))
    padded_dec = jnp.where(inside, joined, jnp.zeros_like(joined))[None]
    return finish(padded_dec, dec_w, dec_b, row_count, col_count)


def solution(mesh):
    placed = (
        P("frame", None, "space", None),
        P(),
        P(),
        P(),
        P(),
        P(None, None, "frame", None),
        P(None, None, "frame", None),
        P(None, None, "frame", None),
        P(None, None, "frame", None),
        P(None, "frame"),
        P(),
        P(),
    )
    return jax.shard_map(
        per_device,
        mesh=mesh,
        in_specs=placed,
        out_specs=P("frame", None, "space", None),
        check_vma=False,
    )
```
